256 devices in a mesh: dp: 16 (over x, y), expert: 16 (over z, core).
Axes of the slice: x: 4, y: 4, z: 8, core: 2. Of those that a mesh axis runs over, the one named last changes fastest.
Arguments:
- hidden: bfloat16 [32768, 8, 768], P(('dp', 'expert')), may hold values from -6 to 6
- upstream: bfloat16 [32768, 4096], P(('dp', 'expert')), may hold values from -0.125 to 0.125
- probs: bfloat16 [32768, 8], P(('dp', 'expert')), may hold values from 0.019897461 to 0.5
- expert_ids: int32 [32768, 8], P(('dp', 'expert')), may hold values from 0 to 15, all different within a row; in each aligned block of 128 rows (0 to 127, 128 to 255, ...) at most 72 rows name the same one
- w_down: bfloat16 [16, 4096, 768], P('expert', 'dp'), may hold values from -0.21875 to 0.21875
Outputs:
- grad_down: float32 [16, 4096, 768], P('expert', 'dp')
- gate_grad: float32 [32768, 8], P(('dp', 'expert'))
The draws below stay inside these ranges and needn't reach their ends.
Inputs may be any that keep to these rules, and one draw needn't show every extreme that they name: `expert_ids`: each row names 8 different experts; among the rows of one device no expert is named by more than 72 rows, a bound that some block reaches.
All inputs are finite; a program needn't handle non-finite values.
Results may differ from the reference program's by a relative error of at most 0.013.
Values may be sent and summed in bfloat16 or wider, within the bound.
No kernel may reach another device: no remote copies, remote signals or barrier semaphores. Data moves between devices by JAX's collectives and lax.ppermute only.
A program may use at most 128 MiB of HBM per device.

```python
import math
import jax
import jax.numpy as jnp
import numpy as np
from jax import lax

D = 4096
HID = 768
TOP = 8
TOK_DEV = 128
EXPERTS = 16
CAP = 72
TOKENS = 32768
N_DP = 16
N_EXPERT = 16


def levels(key, extent, pieces, least, largest):
    def one(dim, shards_of):
        steps = jax.random.uniform(jax.random.fold_in(jax.random.fold_in(key, 6), dim), (shards_of,), jnp.float32, least / len(pieces), largest / len(pieces))
        return jnp.repeat(jnp.exp(steps), extent[dim] // shards_of).reshape((-1,) + (1,) * (len(extent) - dim - 1))

    level = one(*pieces[0])
    for cut in pieces[1:]:
        level = level * one(*cut)
    return level


def shared_out(key, own, number, rows, count, top, limit, lean):
    ranking = jax.random.permutation(key, count)
    heavy_load, ordinary = portions_of(count, rows * top, limit, lean, True), portions_of(count, rows * top, limit, lean, False)
    places = jnp.arange(count)

    def named(tallies, turn):
        used = int((tallies > 0).sum())
        fixed = max(1, used // 4)
        passed = fixed + (places - fixed + turn * (used - fixed)) % max(1, count - fixed)
        return jnp.zeros((count,), jnp.int32).at[ranking[jnp.where(places < fixed, places, passed)]].set(jnp.asarray(tallies, jnp.int32))

    tallies = jnp.where(number % 4 == 0, named(heavy_load, number // 4), named(ordinary, number - number // 4 - 1))
    mixed = jax.random.permutation(jax.random.fold_in(own, 3), count)
    donor, receiver = mixed[0:count // 2 * 2:2], mixed[1:count // 2 * 2:2]
    margin = jnp.minimum(tallies[donor] - 1, limit - tallies[receiver]) // 2
    margin = jnp.where((donor == ranking[0]) | (receiver == ranking[0]) | (tallies[receiver] == 0), 0, jnp.maximum(margin, 0))
    passed = jax.random.randint(jax.random.fold_in(own, 4), (count // 2,), 0, 1 << 20) % (margin + 1)
    tallies = tallies.at[donor].add(-passed).at[receiver].add(passed)
    members = jnp.searchsorted(jnp.cumsum(tallies), jnp.arange(rows * top), side="right").astype(jnp.int32)
    grid = members.reshape(top, rows).T
    grid = grid[jax.random.permutation(jax.random.fold_in(own, 1), rows)]
    turn = jax.random.randint(jax.random.fold_in(own, 2), (rows, 1), 0, top)
    return jnp.take_along_axis(grid, (jnp.arange(top)[None, :] + turn) % top, axis=1)


def portions_of(count, total, limit, slope, full):
    loads = [(1 << 20) // math.isqrt(standing ** slope) + 1 for standing in range(1, count + 1)]
    largest = limit if full else min(limit, max(-(-total // count), total * loads[0] // sum(loads)))
    least = 1 if total - largest >= count - 1 else 0
    given, spare = [largest] + [least] * (count - 1), total - largest - least * (count - 1)
    while spare > 0:
        movable = [i for i in range(1, count) if given[i] < largest] or [i for i in range(1, count) if given[i] < limit]
        pool, left = sum([loads[i] for i in movable]), spare
        for i in movable:
            addition = min(limit - given[i], max(1, left * loads[i] // pool), spare)
            given[i] = given[i] + addition
            spare = spare - addition
    return np.array(given)


def scatter_about(rng, extent, deviation, most, pieces=(), held_as=jnp.bfloat16):
    loudness = levels(rng, extent, pieces, -0.22, 0.18) if pieces else 1.0
    drawn = jax.random.normal(rng, extent, jnp.float32) * deviation * loudness
    return jnp.minimum(jnp.maximum(drawn, -most), most).astype(held_as)


def setup_inputs(seed: int = 0) -> dict:
    seeds = jax.random.split(jax.random.key(seed), 6)
    hidden = scatter_about(seeds[0], (TOKENS, TOP, HID), 1.0, 6.0, ((0, 256),))
    upstream = scatter_about(seeds[1], (TOKENS, D), 0.02, 0.125, ((0, 256),))
    probs = jnp.clip(jnp.exp(math.log(0.5) - 3.224016 * jax.random.uniform(seeds[2], (TOKENS, TOP), jnp.float32) ** levels(seeds[2], (TOKENS, TOP), ((0, 256),), -0.2, 0.2)), 0.019897461, 0.5).astype(jnp.bfloat16)
    expert_ids_keys = jax.random.split(jax.random.fold_in(seeds[3], 1), TOKENS // TOK_DEV)
    expert_ids_turns = jax.random.permutation(jax.random.fold_in(seeds[3], 3), TOKENS // TOK_DEV)
    expert_ids = jax.vmap(lambda own, number: shared_out(jax.random.fold_in(seeds[3], 2), own, number, TOK_DEV, EXPERTS, TOP, CAP, 1))(expert_ids_keys, expert_ids_turns).reshape((TOKENS, TOP))
    w_down = scatter_about(seeds[4], (EXPERTS, D, HID), HID ** -0.5, 0.21875, ((0, 16), (1, 16)))
    return {"hidden": hidden, "upstream": upstream, "probs": probs, "expert_ids": expert_ids, "w_down": w_down}


def reference(hidden, upstream, probs, expert_ids, w_down):
    group_tokens = N_EXPERT * TOK_DEV
    group_slots = group_tokens * TOP
    expert_rows = N_EXPERT * CAP
    hidden_groups = hidden.reshape(N_DP, group_slots, HID)
    upstream_groups = upstream.reshape(N_DP, group_tokens, D)
    prob_groups = probs.reshape(N_DP, group_slots)
    id_groups = expert_ids.reshape(N_DP, group_slots)

    def one_group(running, inputs):
        hidden_slots, upstream_rows, prob_slots, id_slots = inputs

        def one_expert(expert_index):
            slot_order = jnp.argsort((id_slots != expert_index).astype(jnp.int32), stable=True)[:expert_rows].astype(jnp.int32)
            live_slot = id_slots[slot_order] == expert_index
            rows_h = hidden_slots[slot_order]
            rows_dy = upstream_rows[slot_order // TOP]
            projected = jnp.dot(rows_h, w_down[expert_index].T, preferred_element_type=jnp.float32)
            slot_score = jnp.sum(projected * rows_dy.astype(jnp.float32), axis=1)
            weight = jnp.where(live_slot, prob_slots[slot_order].astype(jnp.float32), jnp.float32(0.0))
            scaled = (weight[:, None] * rows_dy.astype(jnp.float32)).astype(jnp.bfloat16)
            partial_value = jnp.dot(scaled.T, rows_h, preferred_element_type=jnp.float32).astype(jnp.bfloat16)
            return partial_value, slot_order, jnp.where(live_slot, slot_score, jnp.float32(0.0))

        partials, orders, scores = lax.map(one_expert, jnp.arange(N_EXPERT, dtype=jnp.int32))
        partials = lax.optimization_barrier(partials)
        slot_grad = jnp.zeros((group_slots,), jnp.float32).at[orders.reshape(-1)].add(scores.reshape(-1))
        return running + partials.astype(jnp.float32), slot_grad

    start_grad = jnp.zeros((N_EXPERT, D, HID), jnp.float32)
    grad_down, slot_grads = lax.scan(one_group, start_grad, (hidden_groups, upstream_groups, prob_groups, id_groups))
    return grad_down, slot_grads.reshape(N_DP * group_tokens, TOP)
```

```python
import jax
import jax.numpy as jnp
from jax import lax
from jax.sharding import PartitionSpec as P


def body(hidden, upstream, probs, expert_ids, w_down):
    tok_rows, top_k = expert_ids.shape
    hid_width = hidden.shape[2]
    groups = lax.axis_size("expert")
    slots_per = max(tok_rows * 9 // 16, tok_rows * top_k // groups)
    total_rows = groups * slots_per
    chosen = (expert_ids[:, :, None] == jnp.arange(groups, dtype=jnp.int32)[None, None, :]).astype(
        jnp.int32
    )
    member = jnp.sum(chosen, axis=1)
    slot_place = jnp.cumsum(member, axis=0) - 1
    which_k = jnp.sum(chosen * jnp.arange(top_k, dtype=jnp.int32)[None, :, None], axis=1)
    target = (
        (member == 1)[:, :, None]
        & (slot_place[:, :, None] == jnp.arange(slots_per, dtype=jnp.int32)[None, None, :])
    ).astype(jnp.int32)
    filled = jnp.sum(target, axis=0) == 1
    source_tok = jnp.sum(target * jnp.arange(tok_rows, dtype=jnp.int32)[:, None, None], axis=0)
    source_k = jnp.sum(target * which_k[:, :, None], axis=0)
    flat_index = (source_tok * top_k + source_k).reshape(-1)
    picked_h = hidden.reshape(tok_rows * top_k, hid_width)[flat_index].reshape(
        groups, slots_per, hid_width
    )
    send_h = jnp.where(filled[:, :, None], picked_h, jnp.zeros_like(picked_h))
    picked_p = probs.reshape(-1)[flat_index].reshape(groups, slots_per)
    send_p = jnp.where(filled, picked_p, jnp.zeros_like(picked_p))
    dy_all = lax.all_gather(upstream, "expert", axis=0, tiled=True)
    recv_h, recv_p, recv_tok = (
        lax.all_to_all(send_h, "expert", split_axis=0, concat_axis=0, tiled=True),
        lax.all_to_all(send_p, "expert", split_axis=0, concat_axis=0, tiled=True),
        lax.all_to_all(source_tok, "expert", split_axis=0, concat_axis=0, tiled=True),
    )
    row_of = recv_tok + tok_rows * jnp.arange(groups, dtype=jnp.int32)[:, None]
    rows_h = recv_h.reshape(total_rows, hid_width)
    rows_dy = dy_all[row_of.reshape(-1)]
    projected = lax.dot_general(
        rows_h,
        lax.all_gather(w_down, "dp", axis=1, tiled=True)[0],
        (((1,), (1,)), ((), ())),
        preferred_element_type=jnp.float32,
    )
    scores = jnp.sum(projected * rows_dy.astype(jnp.float32), axis=1)
    returned = lax.all_to_all(
        scores.reshape(groups, slots_per), "expert", split_axis=0, concat_axis=0, tiled=True
    )
    scaled = (recv_p.reshape(total_rows, 1).astype(jnp.float32) * rows_dy.astype(jnp.float32)).astype(
        jnp.bfloat16
    )
    grad_block = lax.psum_scatter(
        lax.dot_general(
            scaled, rows_h, (((0,), (0,)), ((), ())), preferred_element_type=jnp.float32
        ).astype(jnp.bfloat16),
        "dp",
        scatter_dimension=0,
        tiled=True,
    ).astype(jnp.float32)
    place_slot = jnp.take_along_axis(slot_place, expert_ids, axis=1)
    gate_grad = returned[expert_ids, place_slot]
    return (grad_block[None], gate_grad)


def solution(mesh):
    in_specs = (
        P(("dp", "expert"), None, None),
        P(("dp", "expert"), None),
        P(("dp", "expert"), None),
        P(("dp", "expert"), None),
        P("expert", "dp", None),
    )
    out_specs = (P("expert", "dp", None), P(("dp", "expert"), None))
    return jax.shard_map(body, mesh=mesh, in_specs=in_specs, out_specs=out_specs, check_vma=False)
```

```python
import jax
import jax.numpy as jnp
from jax import lax
from jax.sharding import Mesh, PartitionSpec as P


def body(hidden, upstream, probs, expert_ids, w_down):
    tok_rows, top_k = expert_ids.shape
    hid_width = hidden.shape[2]
    model_width = upstream.shape[1]
    lanes = 128
    n_z = lax.axis_size("z")
    n_core = lax.axis_size("core")
    groups = n_z * n_core
    n_dp = lax.axis_size("dp")
    slots_per = max(tok_rows * 9 // 16, tok_rows * top_k // groups)
    total_rows = groups * slots_per
    chosen = (expert_ids[:, :, None] == jnp.arange(groups, dtype=jnp.int32)[None, None, :]).astype(
        jnp.int32
    )
    member = jnp.sum(chosen, axis=1)
    slot_place = jnp.cumsum(member, axis=0) - 1
    which_k = jnp.sum(chosen * jnp.arange(top_k, dtype=jnp.int32)[None, :, None], axis=1)
    target = (
        (member == 1)[:, :, None]
        & (slot_place[:, :, None] == jnp.arange(slots_per, dtype=jnp.int32)[None, None, :])
    ).astype(jnp.int32)
    filled = jnp.sum(target, axis=0) == 1
    source_tok = jnp.sum(target * jnp.arange(tok_rows, dtype=jnp.int32)[:, None, None], axis=0)
    source_k = jnp.sum(target * which_k[:, :, None], axis=0)
    flat_index = (source_tok * top_k + source_k).reshape(-1)
    picked_h = hidden.reshape(tok_rows * top_k, hid_width)[flat_index].reshape(
        groups, slots_per, hid_width
    )
    send_h = jnp.where(filled[:, :, None], picked_h, jnp.zeros_like(picked_h))
    picked_p = probs.reshape(-1)[flat_index].reshape(groups, slots_per)
    send_p = jnp.where(filled, picked_p, jnp.zeros_like(picked_p))
    dy3 = upstream.reshape(tok_rows, model_width // lanes, lanes)
    dy_z = lax.all_gather(dy3, "z", axis=0, tiled=True)
    dy_pair = lax.ppermute(dy_z, "core", perm=[(c, (c + 1) % n_core) for c in range(n_core)])
    dy_all = jnp.concatenate([dy_z, dy_pair], axis=0)
    w_blocks = lax.all_to_all(
        jnp.broadcast_to(w_down, (n_dp,) + w_down.shape[1:]), "dp", split_axis=0, concat_axis=0, tiled=True
    )
    w_full = w_blocks.reshape(n_dp * w_down.shape[1] // lanes, lanes, hid_width)
    ez = ("z", "core")
    recv_h, recv_p, recv_tok = (
        lax.all_to_all(send_h, ez, split_axis=0, concat_axis=0, tiled=True),
        lax.all_to_all(send_p, ez, split_axis=0, concat_axis=0, tiled=True),
        lax.all_to_all(source_tok, ez, split_axis=0, concat_axis=0, tiled=True),
    )
    src = jnp.arange(groups, dtype=jnp.int32)
    src_z, src_core = src // n_core, src % n_core
    my_core = lax.axis_index("core")
    block = (src_core - my_core + n_core) % n_core
    row_of = recv_tok + (tok_rows * (block * n_z + src_z))[:, None]
    rows_h = recv_h.reshape(total_rows, hid_width)
    rows_dy = dy_all[row_of.reshape(-1)]
    projected = lax.dot_general(
        rows_h, w_full, (((1,), (2,)), ((), ())), preferred_element_type=jnp.float32
    )
    scores = jnp.sum(projected * rows_dy.astype(jnp.float32), axis=(1, 2))
    returned = lax.all_to_all(
        scores.reshape(groups, slots_per), ez, split_axis=0, concat_axis=0, tiled=True
    )
    scaled = (
        recv_p.reshape(total_rows, 1, 1).astype(jnp.float32) * rows_dy.astype(jnp.float32)
    ).astype(jnp.bfloat16)
    partial = lax.dot_general(
        scaled, rows_h, (((0,), (0,)), ((), ())), preferred_element_type=jnp.float32
    ).astype(jnp.bfloat16)
    grad_block = lax.psum_scatter(
        partial.reshape(model_width, hid_width), "dp", scatter_dimension=0, tiled=True
    ).astype(jnp.float32)
    place_slot = jnp.take_along_axis(slot_place, expert_ids, axis=1)
    gate_grad = returned[expert_ids, place_slot]
    return (grad_block[None], gate_grad)


def solution(mesh):
    n_dp, n_expert = mesh.devices.shape
    sub = Mesh(mesh.devices.reshape(n_dp, n_expert // 2, 2), ("dp", "z", "core"))
    tok = ("dp", "z", "core")
    in_specs = (
        P(tok, None, None),
        P(tok, None),
        P(tok, None),
        P(tok, None),
        P(("z", "core"), "dp", None),
    )
    out_specs = (P(("z", "core"), "dp", None), P(tok, None))
    return jax.shard_map(body, mesh=sub, in_specs=in_specs, out_specs=out_specs, check_vma=False)
```

```python
import jax
import jax.numpy as jnp
from jax import lax
from jax.sharding import Mesh, PartitionSpec as P


def body(hidden, upstream, probs, expert_ids, w_down):
    tok_rows, top_k = expert_ids.shape
    hid_width = hidden.shape[2]
    model_width = upstream.shape[1]
    lanes = 128
    n_z = lax.axis_size("z")
    n_core = lax.axis_size("core")
    groups = n_z * n_core
    n_dp = lax.axis_size("dp")
    slots_per = max(tok_rows * 9 // 16, tok_rows * top_k // groups)
    total_rows = groups * slots_per
    chosen = (expert_ids[:, :, None] == jnp.arange(groups, dtype=jnp.int32)[None, None, :]).astype(
        jnp.int32
    )
    member = jnp.sum(chosen, axis=1)
    slot_place = jnp.cumsum(member, axis=0) - 1
    which_k = jnp.sum(chosen * jnp.arange(top_k, dtype=jnp.int32)[None, :, None], axis=1)
    target = (
        (member == 1)[:, :, None]
        & (slot_place[:, :, None] == jnp.arange(slots_per, dtype=jnp.int32)[None, None, :])
    ).astype(jnp.int32)
    filled = jnp.sum(target, axis=0) == 1
    source_tok = jnp.sum(target * jnp.arange(tok_rows, dtype=jnp.int32)[:, None, None], axis=0)
    source_k = jnp.sum(target * which_k[:, :, None], axis=0)
    flat_index = (source_tok * top_k + source_k).reshape(-1)
    picked_h = hidden.reshape(tok_rows * top_k, hid_width)[flat_index].reshape(
        groups, slots_per, hid_width
    )
    send_h = jnp.where(filled[:, :, None], picked_h, jnp.zeros_like(picked_h))
    picked_p = probs.reshape(-1)[flat_index].reshape(groups, slots_per)
    send_p = jnp.where(filled, picked_p, jnp.zeros_like(picked_p))
    dy3 = upstream.reshape(tok_rows, model_width // lanes, lanes)
    dy_z = lax.all_gather(dy3, "z", axis=0, tiled=True)
    w_full = lax.all_gather(w_down, "dp", axis=1, tiled=True)[0]
    ez = ("z", "core")
    recv_h, recv_p, recv_tok = (
        lax.all_to_all(send_h, ez, split_axis=0, concat_axis=0, tiled=True),
        lax.all_to_all(send_p, ez, split_axis=0, concat_axis=0, tiled=True),
        lax.all_to_all(source_tok, ez, split_axis=0, concat_axis=0, tiled=True),
    )
    dy_z, recv_h, recv_p, recv_tok = lax.optimization_barrier((dy_z, recv_h, recv_p, recv_tok))
    dy_pair = lax.ppermute(dy_z, "core", perm=[(c, (c + 1) % n_core) for c in range(n_core)])
    my_core = lax.axis_index("core")
    other_core = (my_core + 1) % n_core
    half = n_z * slots_per

    def side(x, c):
        x = x.reshape((n_z, n_core) + x.shape[1:])
        return lax.dynamic_index_in_dim(x, c, axis=1, keepdims=False)

    z_base = (tok_rows * jnp.arange(n_z, dtype=jnp.int32))[:, None]
    own_rows = (side(recv_tok, my_core) + z_base).reshape(-1)
    pair_rows = (side(recv_tok, other_core) + z_base).reshape(-1)
    rows_dy = jnp.concatenate([dy_z[own_rows], dy_pair[pair_rows]], axis=0).reshape(total_rows, model_width)
    rows_h = jnp.concatenate(
        [side(recv_h, my_core).reshape(half, hid_width), side(recv_h, other_core).reshape(half, hid_width)], axis=0
    )
    rows_p = jnp.concatenate([side(recv_p, my_core).reshape(half), side(recv_p, other_core).reshape(half)])
    projected = lax.dot_general(
        rows_h, w_full, (((1,), (1,)), ((), ())), preferred_element_type=jnp.float32
    )
    scores = jnp.sum(projected * rows_dy.astype(jnp.float32), axis=1)
    own_s, pair_s = scores[:half].reshape(n_z, slots_per), scores[half:].reshape(n_z, slots_per)
    first = jnp.where(my_core == 0, own_s, pair_s)
    second = jnp.where(my_core == 0, pair_s, own_s)
    in_order = jnp.stack([first, second], axis=1).reshape(groups, slots_per)
    returned = lax.all_to_all(in_order, ez, split_axis=0, concat_axis=0, tiled=True)
    scaled = (rows_p.reshape(total_rows, 1).astype(jnp.float32) * rows_dy.astype(jnp.float32)).astype(
        jnp.bfloat16
    )
    partial = lax.dot_general(
        scaled, rows_h, (((0,), (0,)), ((), ())), preferred_element_type=jnp.float32
    ).astype(jnp.bfloat16)
    grad_block = lax.psum_scatter(
        partial, "dp", scatter_dimension=0, tiled=True
    ).astype(jnp.float32)
    place_slot = jnp.take_along_axis(slot_place, expert_ids, axis=1)
    gate_grad = returned[expert_ids, place_slot]
    return (grad_block[None], gate_grad)


def solution(mesh):
    n_dp, n_expert = mesh.devices.shape
    sub = Mesh(mesh.devices.reshape(n_dp, n_expert // 2, 2), ("dp", "z", "core"))
    tok = ("dp", "z", "core")
    in_specs = (
        P(tok, None, None),
        P(tok, None),
        P(tok, None),
        P(tok, None),
        P(("z", "core"), "dp", None),
    )
    out_specs = (P(("z", "core"), "dp", None), P(tok, None))
    return jax.shard_map(body, mesh=sub, in_specs=in_specs, out_specs=out_specs, check_vma=False)
```

```python
import jax
import jax.numpy as jnp
from jax import lax
from jax.sharding import Mesh, PartitionSpec as P


def body(hidden, upstream, probs, expert_ids, w_down):
    tok_rows, top_k = expert_ids.shape
    hid_width = hidden.shape[2]
    model_width = upstream.shape[1]
    n_z = lax.axis_size("z")
    n_core = lax.axis_size("core")
    n_dp = lax.axis_size("dp")
    groups = n_z * n_core
    slots_per = max(tok_rows * 9 // 16, tok_rows * top_k // groups)
    total_rows = groups * slots_per
    ez = ("z", "core")

    chosen = (expert_ids[:, :, None] == jnp.arange(groups, dtype=jnp.int32)[None, None, :]).astype(
        jnp.int32
    )
    member = jnp.sum(chosen, axis=1)
    slot_place = jnp.cumsum(member, axis=0) - 1
    which_k = jnp.sum(chosen * jnp.arange(top_k, dtype=jnp.int32)[None, :, None], axis=1)
    target = (
        (member == 1)[:, :, None]
        & (slot_place[:, :, None] == jnp.arange(slots_per, dtype=jnp.int32)[None, None, :])
    ).astype(jnp.int32)
    filled = jnp.sum(target, axis=0) == 1
    source_tok = jnp.sum(target * jnp.arange(tok_rows, dtype=jnp.int32)[:, None, None], axis=0)
    source_k = jnp.sum(target * which_k[:, :, None], axis=0)
    flat_index = (source_tok * top_k + source_k).reshape(-1)
    picked_h = hidden.reshape(tok_rows * top_k, hid_width)[flat_index].reshape(
        groups, slots_per, hid_width
    )
    send_h = jnp.where(filled[:, :, None], picked_h, jnp.zeros_like(picked_h))
    routed = member == 1
    p_tok = jnp.where(
        routed, jnp.take_along_axis(probs, which_k, axis=1).astype(jnp.float32), jnp.float32(0.0)
    )
    inv = jnp.where(routed, slot_place, -1).astype(jnp.float32)
    send_meta = jnp.stack([p_tok.T, inv.T], axis=1)

    dy_z = lax.all_gather(upstream, "z", axis=0, tiled=True)
    w_blocks = lax.all_to_all(
        jnp.broadcast_to(w_down, (n_dp,) + w_down.shape[1:]), "dp", split_axis=0, concat_axis=0, tiled=True
    )
    w_full = w_blocks.reshape(n_dp * w_down.shape[1], hid_width)
    dy_z, w_full, send_h, send_meta = lax.optimization_barrier((dy_z, w_full, send_h, send_meta))
    dy_pair = lax.ppermute(dy_z, "core", perm=[(c, (c + 1) % n_core) for c in range(n_core)])
    recv_h = lax.all_to_all(send_h, ez, split_axis=0, concat_axis=0, tiled=True)
    recv_meta = lax.all_to_all(send_meta, ez, split_axis=0, concat_axis=0, tiled=True)

    my_core = lax.axis_index("core")
    flat_h = recv_h.reshape(total_rows, hid_width)

    def half(dy_c, c):
        meta = lax.dynamic_index_in_dim(
            recv_meta.reshape(n_z, n_core, 2, tok_rows), c, axis=1, keepdims=False
        )
        p_c = meta[:, 0, :].reshape(-1)
        slot = meta[:, 1, :].astype(jnp.int32)
        live = (slot >= 0).reshape(-1)
        src = (jnp.arange(n_z, dtype=jnp.int32) * n_core + c)[:, None]
        row = (src * slots_per + jnp.maximum(slot, 0)).reshape(-1)
        h_c = jnp.where(live[:, None], flat_h[row], jnp.zeros((), flat_h.dtype))
        scaled = (p_c[:, None] * dy_c.astype(jnp.float32)).astype(jnp.bfloat16)
        part = lax.dot_general(
            scaled, h_c, (((0,), (0,)), ((), ())), preferred_element_type=jnp.float32
        )
        g = lax.dot_general(dy_c, w_full, (((1,), (0,)), ((), ())), preferred_element_type=jnp.float32)
        score = jnp.sum(g * h_c.astype(jnp.float32), axis=1)
        return part, score.reshape(n_z, tok_rows)

    part_own, score_own = half(dy_z, my_core)
    part_pair, score_pair = half(dy_pair, (my_core + 1) % n_core)
    partial = (part_own + part_pair).astype(jnp.bfloat16)
    grad_block = lax.psum_scatter(partial, "dp", scatter_dimension=0, tiled=True).astype(jnp.float32)

    first = jnp.where(my_core == 0, score_own, score_pair)
    second = jnp.where(my_core == 0, score_pair, score_own)
    by_source = jnp.stack([first, second], axis=1).reshape(groups, tok_rows)
    returned = lax.all_to_all(by_source, ez, split_axis=0, concat_axis=0, tiled=True)
    gate_grad = jnp.take_along_axis(returned.T, expert_ids, axis=1)
    return (grad_block[None], gate_grad)


def solution(mesh):
    n_dp, n_expert = mesh.devices.shape
    sub = Mesh(mesh.devices.reshape(n_dp, n_expert // 2, 2), ("dp", "z", "core"))
    tok = ("dp", "z", "core")
    in_specs = (
        P(tok, None, None),
        P(tok, None),
        P(tok, None),
        P(tok, None),
        P(("z", "core"), "dp", None),
    )
    out_specs = (P(("z", "core"), "dp", None), P(tok, None))
    return jax.shard_map(body, mesh=sub, in_specs=in_specs, out_specs=out_specs, check_vma=False)
```

```python
import jax
import jax.numpy as jnp
from jax import lax
from jax.sharding import Mesh, PartitionSpec as P


def body(hidden, upstream, probs, expert_ids, w_down):
    tok_rows, top_k = expert_ids.shape
    hid_width = hidden.shape[2]
    model_width = upstream.shape[1]
    n_z = lax.axis_size("z")
    n_core = lax.axis_size("core")
    n_dp = lax.axis_size("dp")
    groups = n_z * n_core
    slots_per = max(tok_rows * 9 // 16, tok_rows * top_k // groups)
    total_rows = groups * slots_per
    ez = ("z", "core")

    chosen = (expert_ids[:, :, None] == jnp.arange(groups, dtype=jnp.int32)[None, None, :]).astype(
        jnp.int32
    )
    member = jnp.sum(chosen, axis=1)
    slot_place = jnp.cumsum(member, axis=0) - 1
    which_k = jnp.sum(chosen * jnp.arange(top_k, dtype=jnp.int32)[None, :, None], axis=1)
    target = (
        (member == 1)[:, :, None]
        & (slot_place[:, :, None] == jnp.arange(slots_per, dtype=jnp.int32)[None, None, :])
    ).astype(jnp.int32)
    filled = jnp.sum(target, axis=0) == 1
    source_tok = jnp.sum(target * jnp.arange(tok_rows, dtype=jnp.int32)[:, None, None], axis=0)
    source_k = jnp.sum(target * which_k[:, :, None], axis=0)
    flat_index = (source_tok * top_k + source_k).reshape(-1)
    picked_h = hidden.reshape(tok_rows * top_k, hid_width)[flat_index].reshape(
        groups, slots_per, hid_width
    )
    send_h = jnp.where(filled[:, :, None], picked_h, jnp.zeros_like(picked_h))
    routed = member == 1
    p_tok = jnp.where(
        routed, jnp.take_along_axis(probs, which_k, axis=1).astype(jnp.float32), jnp.float32(0.0)
    )
    inv = jnp.where(routed, slot_place, -1).astype(jnp.float32)
    send_meta = jnp.stack([p_tok.T, inv.T], axis=1)

    w_full = lax.all_gather(w_down, "dp", axis=1, tiled=True)[0]
    recv_h = lax.all_to_all(send_h, ez, split_axis=0, concat_axis=0, tiled=True)
    recv_meta = lax.all_to_all(send_meta, ez, split_axis=0, concat_axis=0, tiled=True)
    upstream, w_full, recv_h, recv_meta = lax.optimization_barrier((upstream, w_full, recv_h, recv_meta))
    dy_z = lax.all_gather(upstream, "z", axis=0, tiled=True)
    dy_pair = lax.ppermute(dy_z, "core", perm=[(c, (c + 1) % n_core) for c in range(n_core)])

    my_core = lax.axis_index("core")
    flat_h = recv_h.reshape(total_rows, hid_width)

    def half(dy_c, c):
        meta = lax.dynamic_index_in_dim(
            recv_meta.reshape(n_z, n_core, 2, tok_rows), c, axis=1, keepdims=False
        )
        p_c = meta[:, 0, :].reshape(-1)
        slot = meta[:, 1, :].astype(jnp.int32)
        live = (slot >= 0).reshape(-1)
        src = (jnp.arange(n_z, dtype=jnp.int32) * n_core + c)[:, None]
        row = (src * slots_per + jnp.maximum(slot, 0)).reshape(-1)
        h_c = jnp.where(live[:, None], flat_h[row], jnp.zeros((), flat_h.dtype))
        scaled = (p_c[:, None] * dy_c.astype(jnp.float32)).astype(jnp.bfloat16)
        part = lax.dot_general(
            scaled, h_c, (((0,), (0,)), ((), ())), preferred_element_type=jnp.float32
        )
        g = lax.dot_general(dy_c, w_full, (((1,), (0,)), ((), ())), preferred_element_type=jnp.float32)
        score = jnp.sum(g * h_c.astype(jnp.float32), axis=1)
        return part, score.reshape(n_z, tok_rows)

    part_own, score_own = half(dy_z, my_core)
    part_pair, score_pair = half(dy_pair, (my_core + 1) % n_core)
    partial = (part_own + part_pair).astype(jnp.bfloat16)
    grad_block = lax.psum_scatter(partial, "dp", scatter_dimension=0, tiled=True).astype(jnp.float32)

    first = jnp.where(my_core == 0, score_own, score_pair)
    second = jnp.where(my_core == 0, score_pair, score_own)
    by_source = jnp.stack([first, second], axis=1).reshape(groups, tok_rows)
    returned = lax.all_to_all(by_source, ez, split_axis=0, concat_axis=0, tiled=True)
    gate_grad = jnp.take_along_axis(returned.T, expert_ids, axis=1)
    return (grad_block[None], gate_grad)


def solution(mesh):
    n_dp, n_expert = mesh.devices.shape
    sub = Mesh(mesh.devices.reshape(n_dp, n_expert // 2, 2), ("dp", "z", "core"))
    tok = ("dp", "z", "core")
    in_specs = (
        P(tok, None, None),
        P(tok, None),
        P(tok, None),
        P(tok, None),
        P(("z", "core"), "dp", None),
    )
    out_specs = (P(("z", "core"), "dp", None), P(tok, None))
    return jax.shard_map(body, mesh=sub, in_specs=in_specs, out_specs=out_specs, check_vma=False)
```

```python
import jax
import jax.numpy as jnp
from jax import lax
from jax.sharding import Mesh, PartitionSpec as P


def body(hidden, upstream, probs, expert_ids, w_down):
    tok_rows, top_k = expert_ids.shape
    hid_width = hidden.shape[2]
    model_width = upstream.shape[1]
    n_z = lax.axis_size("z")
    n_core = lax.axis_size("core")
    n_dp = lax.axis_size("dp")
    groups = n_z * n_core
    slots_per = max(tok_rows * 9 // 16, tok_rows * top_k // groups)
    total_rows = groups * slots_per
    ez = ("z", "core")

    chosen = (expert_ids[:, :, None] == jnp.arange(groups, dtype=jnp.int32)[None, None, :]).astype(
        jnp.int32
    )
    member = jnp.sum(chosen, axis=1)
    slot_place = jnp.cumsum(member, axis=0) - 1
    which_k = jnp.sum(chosen * jnp.arange(top_k, dtype=jnp.int32)[None, :, None], axis=1)
    target = (
        (member == 1)[:, :, None]
        & (slot_place[:, :, None] == jnp.arange(slots_per, dtype=jnp.int32)[None, None, :])
    ).astype(jnp.int32)
    filled = jnp.sum(target, axis=0) == 1
    source_tok = jnp.sum(target * jnp.arange(tok_rows, dtype=jnp.int32)[:, None, None], axis=0)
    source_k = jnp.sum(target * which_k[:, :, None], axis=0)
    flat_index = (source_tok * top_k + source_k).reshape(-1)
    picked_h = hidden.reshape(tok_rows * top_k, hid_width)[flat_index].reshape(
        groups, slots_per, hid_width
    )
    send_h = jnp.where(filled[:, :, None], picked_h, jnp.zeros_like(picked_h))
    routed = member == 1
    p_tok = jnp.sum(
        jnp.where(chosen == 1, probs.astype(jnp.float32)[:, :, None], jnp.float32(0.0)), axis=1
    )
    inv = jnp.where(routed, slot_place, -1).astype(jnp.float32)
    send_meta = jnp.stack([p_tok.T, inv.T], axis=1)

    w_full = lax.all_gather(w_down, "dp", axis=1, tiled=True)[0]
    recv_h = lax.all_to_all(send_h, ez, split_axis=0, concat_axis=0, tiled=True)
    recv_meta = lax.all_to_all(send_meta, ez, split_axis=0, concat_axis=0, tiled=True)
    upstream, w_full, recv_h, recv_meta = lax.optimization_barrier((upstream, w_full, recv_h, recv_meta))
    dy_z = lax.all_gather(upstream, "z", axis=0, tiled=True)
    dy_pair = lax.ppermute(dy_z, "core", perm=[(c, (c + 1) % n_core) for c in range(n_core)])

    my_core = lax.axis_index("core")
    other_core = (my_core + 1) % n_core
    half_hid = hid_width // 2

    def inputs(c):
        meta = lax.dynamic_index_in_dim(
            recv_meta.reshape(n_z, n_core, 2, tok_rows), c, axis=1, keepdims=False
        )
        p_c = meta[:, 0, :].reshape(-1)
        slot = meta[:, 1, :].astype(jnp.int32)
        h_src = lax.dynamic_index_in_dim(
            recv_h.reshape(n_z, n_core, slots_per, hid_width), c, axis=1, keepdims=False
        )
        pick = (slot[:, :, None] == jnp.arange(slots_per, dtype=jnp.int32)[None, None, :]).astype(
            h_src.dtype
        )
        h_c = lax.dot_general(
            pick, h_src, (((2,), (1,)), ((0,), (0,))), preferred_element_type=jnp.float32
        ).astype(h_src.dtype)
        return p_c, h_c.reshape(n_z * tok_rows, hid_width)

    p_own, h_own = inputs(my_core)
    p_pair, h_pair = inputs(other_core)

    def part(dy_c, p_c, h_c, which):
        scaled = (p_c[:, None] * dy_c.astype(jnp.float32)).astype(jnp.bfloat16)
        h_cols = h_c[:, which * half_hid:(which + 1) * half_hid]
        return lax.dot_general(scaled, h_cols, (((0,), (0,)), ((), ())), preferred_element_type=jnp.float32)

    def score(dy_c, h_c):
        g = lax.dot_general(dy_c, w_full, (((1,), (0,)), ((), ())), preferred_element_type=jnp.float32)
        return jnp.sum(g * h_c.astype(jnp.float32), axis=1).reshape(n_z, tok_rows)

    pieces = []
    for which in range(2):
        total = part(dy_z, p_own, h_own, which) + part(dy_pair, p_pair, h_pair, which)
        pieces.append(
            lax.psum_scatter(total.astype(jnp.bfloat16), "dp", scatter_dimension=0, tiled=True)
        )
    grad_block = jnp.concatenate(pieces, axis=1).astype(jnp.float32)
    score_own = score(dy_z, h_own)
    score_pair = score(dy_pair, h_pair)

    first = jnp.where(my_core == 0, score_own, score_pair)
    second = jnp.where(my_core == 0, score_pair, score_own)
    by_source = jnp.stack([first, second], axis=1).reshape(groups, tok_rows)
    returned = lax.all_to_all(by_source, ez, split_axis=0, concat_axis=0, tiled=True)
    gate_grad = jnp.sum(
        jnp.where(
            expert_ids[:, :, None] == jnp.arange(groups, dtype=jnp.int32)[None, None, :],
            returned.T[:, None, :],
            jnp.float32(0.0),
        ),
        axis=2,
    )
    return (grad_block[None], gate_grad)


def solution(mesh):
    n_dp, n_expert = mesh.devices.shape
    sub = Mesh(mesh.devices.reshape(n_dp, n_expert // 2, 2), ("dp", "z", "core"))
    tok = ("dp", "z", "core")
    in_specs = (
        P(tok, None, None),
        P(tok, None),
        P(tok, None),
        P(tok, None),
        P(("z", "core"), "dp", None),
    )
    out_specs = (P(("z", "core"), "dp", None), P(tok, None))
    return jax.shard_map(body, mesh=sub, in_specs=in_specs, out_specs=out_specs, check_vma=False)
```

```python
import jax
import jax.numpy as jnp
from jax import lax
from jax.sharding import Mesh, PartitionSpec as P


def body(hidden, upstream, probs, expert_ids, w_down):
    tok_rows, top_k = expert_ids.shape
    hid_width = hidden.shape[2]
    model_width = upstream.shape[1]
    n_z = lax.axis_size("z")
    n_core = lax.axis_size("core")
    n_dp = lax.axis_size("dp")
    groups = n_z * n_core
    slots_per = max(tok_rows * 9 // 16, tok_rows * top_k // groups)
    total_rows = groups * slots_per
    ez = ("z", "core")

    chosen = (expert_ids[:, :, None] == jnp.arange(groups, dtype=jnp.int32)[None, None, :]).astype(
        jnp.int32
    )
    member = jnp.sum(chosen, axis=1)
    slot_place = jnp.cumsum(member, axis=0) - 1
    which_k = jnp.sum(chosen * jnp.arange(top_k, dtype=jnp.int32)[None, :, None], axis=1)
    target = (
        (member == 1)[:, :, None]
        & (slot_place[:, :, None] == jnp.arange(slots_per, dtype=jnp.int32)[None, None, :])
    ).astype(jnp.int32)
    filled = jnp.sum(target, axis=0) == 1
    source_tok = jnp.sum(target * jnp.arange(tok_rows, dtype=jnp.int32)[:, None, None], axis=0)
    source_k = jnp.sum(target * which_k[:, :, None], axis=0)
    flat_index = (source_tok * top_k + source_k).reshape(-1)
    picked_h = hidden.reshape(tok_rows * top_k, hid_width)[flat_index].reshape(
        groups, slots_per, hid_width
    )
    send_h = jnp.where(filled[:, :, None], picked_h, jnp.zeros_like(picked_h))
    routed = member == 1
    p_tok = jnp.sum(
        jnp.where(chosen == 1, probs.astype(jnp.float32)[:, :, None], jnp.float32(0.0)), axis=1
    )
    inv = jnp.where(routed, slot_place, -1).astype(jnp.float32)
    send_meta = jnp.stack([p_tok.T, inv.T], axis=1)

    w_full = lax.all_gather(w_down, "dp", axis=1, tiled=True)[0]
    recv_h = lax.all_to_all(send_h, ez, split_axis=0, concat_axis=0, tiled=True)
    recv_meta = lax.all_to_all(send_meta, ez, split_axis=0, concat_axis=0, tiled=True)
    upstream, w_full, recv_h, recv_meta = lax.optimization_barrier((upstream, w_full, recv_h, recv_meta))
    dy_z = lax.all_gather(upstream, "z", axis=0, tiled=True)
    dy_pair = lax.ppermute(dy_z, "core", perm=[(c, (c + 1) % n_core) for c in range(n_core)])

    my_core = lax.axis_index("core")
    other_core = (my_core + 1) % n_core

    def inputs(c):
        meta = lax.dynamic_index_in_dim(
            recv_meta.reshape(n_z, n_core, 2, tok_rows), c, axis=1, keepdims=False
        )
        p_c = meta[:, 0, :].reshape(-1)
        slot = meta[:, 1, :].astype(jnp.int32)
        h_src = lax.dynamic_index_in_dim(
            recv_h.reshape(n_z, n_core, slots_per, hid_width), c, axis=1, keepdims=False
        )
        pick = (slot[:, :, None] == jnp.arange(slots_per, dtype=jnp.int32)[None, None, :]).astype(
            h_src.dtype
        )
        h_c = lax.dot_general(
            pick, h_src, (((2,), (1,)), ((0,), (0,))), preferred_element_type=jnp.float32
        ).astype(h_src.dtype)
        return p_c, h_c.reshape(n_z * tok_rows, hid_width)

    p_own, h_own = inputs(my_core)
    p_pair, h_pair = inputs(other_core)

    def part(dy_c, p_c, h_c):
        scaled = (p_c[:, None] * dy_c.astype(jnp.float32)).astype(jnp.bfloat16)
        return lax.dot_general(scaled, h_c, (((0,), (0,)), ((), ())), preferred_element_type=jnp.float32)

    def score(dy_c, h_c):
        g = lax.dot_general(dy_c, w_full, (((1,), (0,)), ((), ())), preferred_element_type=jnp.float32)
        return jnp.sum(g * h_c.astype(jnp.float32), axis=1).reshape(n_z, tok_rows)

    partial = (part(dy_z, p_own, h_own) + part(dy_pair, p_pair, h_pair)).astype(jnp.bfloat16)
    grad_block = lax.psum_scatter(partial, "dp", scatter_dimension=0, tiled=True).astype(jnp.float32)
    score_own = score(dy_z, h_own)
    score_pair = score(dy_pair, h_pair)

    first = jnp.where(my_core == 0, score_own, score_pair)
    second = jnp.where(my_core == 0, score_pair, score_own)
    by_source = jnp.stack([first, second], axis=1).reshape(groups, tok_rows)
    returned = lax.all_to_all(by_source, ez, split_axis=0, concat_axis=0, tiled=True)
    gate_grad = jnp.sum(
        jnp.where(
            expert_ids[:, :, None] == jnp.arange(groups, dtype=jnp.int32)[None, None, :],
            returned.T[:, None, :],
            jnp.float32(0.0),
        ),
        axis=2,
    )
    return (grad_block[None], gate_grad)


def solution(mesh):
    n_dp, n_expert = mesh.devices.shape
    sub = Mesh(mesh.devices.reshape(n_dp, n_expert // 2, 2), ("dp", "z", "core"))
    tok = ("dp", "z", "core")
    in_specs = (
        P(tok, None, None),
        P(tok, None),
        P(tok, None),
        P(tok, None),
        P(("z", "core"), "dp", None),
    )
    out_specs = (P(("z", "core"), "dp", None), P(tok, None))
    return jax.shard_map(body, mesh=sub, in_specs=in_specs, out_specs=out_specs, check_vma=False)
```

```python
import jax
import jax.numpy as jnp
from jax import lax
from jax.sharding import Mesh, PartitionSpec as P


def body(hidden, upstream, probs, expert_ids, w_down):
    tok_rows, top_k = expert_ids.shape
    hid_width = hidden.shape[2]
    model_width = upstream.shape[1]
    n_z = lax.axis_size("z")
    n_core = lax.axis_size("core")
    n_dp = lax.axis_size("dp")
    groups = n_z * n_core
    slots_per = max(tok_rows * 9 // 16, tok_rows * top_k // groups)
    total_rows = groups * slots_per
    ez = ("z", "core")

    chosen = (expert_ids[:, :, None] == jnp.arange(groups, dtype=jnp.int32)[None, None, :]).astype(
        jnp.int32
    )
    member = jnp.sum(chosen, axis=1)
    slot_place = jnp.cumsum(member, axis=0) - 1
    which_k = jnp.sum(chosen * jnp.arange(top_k, dtype=jnp.int32)[None, :, None], axis=1)
    target = (
        (member == 1)[:, :, None]
        & (slot_place[:, :, None] == jnp.arange(slots_per, dtype=jnp.int32)[None, None, :])
    ).astype(jnp.int32)
    filled = jnp.sum(target, axis=0) == 1
    source_tok = jnp.sum(target * jnp.arange(tok_rows, dtype=jnp.int32)[:, None, None], axis=0)
    source_k = jnp.sum(target * which_k[:, :, None], axis=0)
    flat_index = (source_tok * top_k + source_k).reshape(-1)
    picked_h = hidden.reshape(tok_rows * top_k, hid_width)[flat_index].reshape(
        groups, slots_per, hid_width
    )
    send_h = jnp.where(filled[:, :, None], picked_h, jnp.zeros_like(picked_h))
    routed = member == 1
    p_tok = jnp.sum(
        jnp.where(chosen == 1, probs.astype(jnp.float32)[:, :, None], jnp.float32(0.0)), axis=1
    )
    inv = jnp.where(routed, slot_place, -1).astype(jnp.float32)
    send_meta = jnp.stack([p_tok.T, inv.T], axis=1)

    dy_z = lax.all_gather(upstream, "z", axis=0, tiled=True)
    recv_h = lax.all_to_all(send_h, ez, split_axis=0, concat_axis=0, tiled=True)
    recv_meta = lax.all_to_all(send_meta, ez, split_axis=0, concat_axis=0, tiled=True)
    n_cut = 8
    cut = hid_width // n_cut
    w_full = jnp.concatenate(
        [
            lax.all_gather(w_down[0, :, i * cut:(i + 1) * cut], "dp", axis=0, tiled=True)
            for i in range(n_cut)
        ],
        axis=1,
    )
    dy_z, w_full, recv_h, recv_meta = lax.optimization_barrier((dy_z, w_full, recv_h, recv_meta))
    dy_pair = lax.ppermute(dy_z, "core", perm=[(c, (c + 1) % n_core) for c in range(n_core)])

    my_core = lax.axis_index("core")
    other_core = (my_core + 1) % n_core

    def inputs(c):
        meta = lax.dynamic_index_in_dim(
            recv_meta.reshape(n_z, n_core, 2, tok_rows), c, axis=1, keepdims=False
        )
        p_c = meta[:, 0, :].reshape(-1)
        slot = meta[:, 1, :].astype(jnp.int32)
        h_src = lax.dynamic_index_in_dim(
            recv_h.reshape(n_z, n_core, slots_per, hid_width), c, axis=1, keepdims=False
        )
        pick = (slot[:, :, None] == jnp.arange(slots_per, dtype=jnp.int32)[None, None, :]).astype(
            h_src.dtype
        )
        h_c = lax.dot_general(
            pick, h_src, (((2,), (1,)), ((0,), (0,))), preferred_element_type=jnp.float32
        ).astype(h_src.dtype)
        return p_c, h_c.reshape(n_z * tok_rows, hid_width)

    p_own, h_own = inputs(my_core)
    p_pair, h_pair = inputs(other_core)

    def part(dy_c, p_c, h_c):
        scaled = (p_c[:, None] * dy_c.astype(jnp.float32)).astype(jnp.bfloat16)
        return lax.dot_general(scaled, h_c, (((0,), (0,)), ((), ())), preferred_element_type=jnp.float32)

    def score(dy_c, h_c):
        g = lax.dot_general(dy_c, w_full, (((1,), (0,)), ((), ())), preferred_element_type=jnp.float32)
        return jnp.sum(g * h_c.astype(jnp.float32), axis=1).reshape(n_z, tok_rows)

    partial = (part(dy_z, p_own, h_own) + part(dy_pair, p_pair, h_pair)).astype(jnp.bfloat16)
    grad_block = lax.psum_scatter(partial, "dp", scatter_dimension=0, tiled=True).astype(jnp.float32)
    score_own = score(dy_z, h_own)
    score_pair = score(dy_pair, h_pair)

    first = jnp.where(my_core == 0, score_own, score_pair)
    second = jnp.where(my_core == 0, score_pair, score_own)
    by_source = jnp.stack([first, second], axis=1).reshape(groups, tok_rows)
    returned = lax.all_to_all(by_source, ez, split_axis=0, concat_axis=0, tiled=True)
    gate_grad = jnp.sum(
        jnp.where(
            expert_ids[:, :, None] == jnp.arange(groups, dtype=jnp.int32)[None, None, :],
            returned.T[:, None, :],
            jnp.float32(0.0),
        ),
        axis=2,
    )
    return (grad_block[None], gate_grad)


def solution(mesh):
    n_dp, n_expert = mesh.devices.shape
    sub = Mesh(mesh.devices.reshape(n_dp, n_expert // 2, 2), ("dp", "z", "core"))
    tok = ("dp", "z", "core")
    in_specs = (
        P(tok, None, None),
        P(tok, None),
        P(tok, None),
        P(tok, None),
        P(("z", "core"), "dp", None),
    )
    out_specs = (P(("z", "core"), "dp", None), P(tok, None))
    return jax.shard_map(body, mesh=sub, in_specs=in_specs, out_specs=out_specs, check_vma=False)
```

```python
import jax
import jax.numpy as jnp
from jax import lax
from jax.sharding import Mesh, PartitionSpec as P


def body(hidden, upstream, probs, expert_ids, w_down):
    tok_rows, top_k = expert_ids.shape
    hid_width = hidden.shape[2]
    model_width = upstream.shape[1]
    n_z = lax.axis_size("z")
    n_core = lax.axis_size("core")
    n_dp = lax.axis_size("dp")
    groups = n_z * n_core
    slots_per = max(tok_rows * 9 // 16, tok_rows * top_k // groups)
    total_rows = groups * slots_per
    ez = ("z", "core")

    chosen = (expert_ids[:, :, None] == jnp.arange(groups, dtype=jnp.int32)[None, None, :]).astype(
        jnp.int32
    )
    member = jnp.sum(chosen, axis=1)
    slot_place = jnp.cumsum(member, axis=0) - 1
    which_k = jnp.sum(chosen * jnp.arange(top_k, dtype=jnp.int32)[None, :, None], axis=1)
    target = (
        (member == 1)[:, :, None]
        & (slot_place[:, :, None] == jnp.arange(slots_per, dtype=jnp.int32)[None, None, :])
    ).astype(jnp.int32)
    filled = jnp.sum(target, axis=0) == 1
    source_tok = jnp.sum(target * jnp.arange(tok_rows, dtype=jnp.int32)[:, None, None], axis=0)
    source_k = jnp.sum(target * which_k[:, :, None], axis=0)
    flat_index = (source_tok * top_k + source_k).reshape(-1)
    picked_h = hidden.reshape(tok_rows * top_k, hid_width)[flat_index].reshape(
        groups, slots_per, hid_width
    )
    send_h = jnp.where(filled[:, :, None], picked_h, jnp.zeros_like(picked_h))
    routed = member == 1
    p_tok = jnp.sum(
        jnp.where(chosen == 1, probs.astype(jnp.float32)[:, :, None], jnp.float32(0.0)), axis=1
    )
    inv = jnp.where(routed, slot_place, -1).astype(jnp.float32)
    send_meta = jnp.stack([p_tok.T, inv.T], axis=1)

    dy_z = lax.all_gather(upstream, "z", axis=0, tiled=True)
    recv_h = lax.all_to_all(send_h, ez, split_axis=0, concat_axis=0, tiled=True)
    recv_meta = lax.all_to_all(send_meta, ez, split_axis=0, concat_axis=0, tiled=True)
    w_pieces = [w_down[0]] + [
        lax.ppermute(w_down[0], "dp", perm=[(i, (i - d) % n_dp) for i in range(n_dp)])
        for d in range(1, n_dp)
    ]
    w_full = jnp.stack(w_pieces)
    dy_z, w_full, recv_h, recv_meta = lax.optimization_barrier((dy_z, w_full, recv_h, recv_meta))
    w_full = jnp.roll(w_full, lax.axis_index("dp"), axis=0).reshape(-1, hid_width)
    dy_pair = lax.ppermute(dy_z, "core", perm=[(c, (c + 1) % n_core) for c in range(n_core)])

    my_core = lax.axis_index("core")
    other_core = (my_core + 1) % n_core

    def inputs(c):
        meta = lax.dynamic_index_in_dim(
            recv_meta.reshape(n_z, n_core, 2, tok_rows), c, axis=1, keepdims=False
        )
        p_c = meta[:, 0, :].reshape(-1)
        slot = meta[:, 1, :].astype(jnp.int32)
        h_src = lax.dynamic_index_in_dim(
            recv_h.reshape(n_z, n_core, slots_per, hid_width), c, axis=1, keepdims=False
        )
        pick = (slot[:, :, None] == jnp.arange(slots_per, dtype=jnp.int32)[None, None, :]).astype(
            h_src.dtype
        )
        h_c = lax.dot_general(
            pick, h_src, (((2,), (1,)), ((0,), (0,))), preferred_element_type=jnp.float32
        ).astype(h_src.dtype)
        return p_c, h_c.reshape(n_z * tok_rows, hid_width)

    p_own, h_own = inputs(my_core)
    p_pair, h_pair = inputs(other_core)

    def part(dy_c, p_c, h_c):
        scaled = (p_c[:, None] * dy_c.astype(jnp.float32)).astype(jnp.bfloat16)
        return lax.dot_general(scaled, h_c, (((0,), (0,)), ((), ())), preferred_element_type=jnp.float32)

    def score(dy_c, h_c):
        g = lax.dot_general(dy_c, w_full, (((1,), (0,)), ((), ())), preferred_element_type=jnp.float32)
        return jnp.sum(g * h_c.astype(jnp.float32), axis=1).reshape(n_z, tok_rows)

    partial = (part(dy_z, p_own, h_own) + part(dy_pair, p_pair, h_pair)).astype(jnp.bfloat16)
    grad_block = lax.psum_scatter(partial, "dp", scatter_dimension=0, tiled=True).astype(jnp.float32)
    score_own = score(dy_z, h_own)
    score_pair = score(dy_pair, h_pair)

    first = jnp.where(my_core == 0, score_own, score_pair)
    second = jnp.where(my_core == 0, score_pair, score_own)
    by_source = jnp.stack([first, second], axis=1).reshape(groups, tok_rows)
    returned = lax.all_to_all(by_source, ez, split_axis=0, concat_axis=0, tiled=True)
    gate_grad = jnp.sum(
        jnp.where(
            expert_ids[:, :, None] == jnp.arange(groups, dtype=jnp.int32)[None, None, :],
            returned.T[:, None, :],
            jnp.float32(0.0),
        ),
        axis=2,
    )
    return (grad_block[None], gate_grad)


def solution(mesh):
    n_dp, n_expert = mesh.devices.shape
    sub = Mesh(mesh.devices.reshape(n_dp, n_expert // 2, 2), ("dp", "z", "core"))
    tok = ("dp", "z", "core")
    in_specs = (
        P(tok, None, None),
        P(tok, None),
        P(tok, None),
        P(tok, None),
        P(("z", "core"), "dp", None),
    )
    out_specs = (P(("z", "core"), "dp", None), P(tok, None))
    return jax.shard_map(body, mesh=sub, in_specs=in_specs, out_specs=out_specs, check_vma=False)
```

```python
import jax
import jax.numpy as jnp
from jax import lax
from jax.sharding import Mesh, PartitionSpec as P


def body(hidden, upstream, probs, expert_ids, w_down):
    tok_rows, top_k = expert_ids.shape
    hid_width = hidden.shape[2]
    model_width = upstream.shape[1]
    n_z = lax.axis_size("z")
    n_core = lax.axis_size("core")
    n_dp = lax.axis_size("dp")
    groups = n_z * n_core
    slots_per = max(tok_rows * 9 // 16, tok_rows * top_k // groups)
    total_rows = groups * slots_per
    ez = ("z", "core")

    chosen = (expert_ids[:, :, None] == jnp.arange(groups, dtype=jnp.int32)[None, None, :]).astype(
        jnp.int32
    )
    member = jnp.sum(chosen, axis=1)
    slot_place = jnp.cumsum(member, axis=0) - 1
    which_k = jnp.sum(chosen * jnp.arange(top_k, dtype=jnp.int32)[None, :, None], axis=1)
    target = (
        (member == 1)[:, :, None]
        & (slot_place[:, :, None] == jnp.arange(slots_per, dtype=jnp.int32)[None, None, :])
    ).astype(jnp.int32)
    filled = jnp.sum(target, axis=0) == 1
    source_tok = jnp.sum(target * jnp.arange(tok_rows, dtype=jnp.int32)[:, None, None], axis=0)
    source_k = jnp.sum(target * which_k[:, :, None], axis=0)
    flat_index = (source_tok * top_k + source_k).reshape(-1)
    picked_h = hidden.reshape(tok_rows * top_k, hid_width)[flat_index].reshape(
        groups, slots_per, hid_width
    )
    send_h = jnp.where(filled[:, :, None], picked_h, jnp.zeros_like(picked_h))
    routed = member == 1
    p_tok = jnp.sum(
        jnp.where(chosen == 1, probs.astype(jnp.float32)[:, :, None], jnp.float32(0.0)), axis=1
    )
    inv = jnp.where(routed, slot_place, -1).astype(jnp.float32)
    send_meta = jnp.stack([p_tok.T, inv.T], axis=1)

    dy_z = lax.all_gather(upstream, "z", axis=0, tiled=True)
    recv_h = lax.all_to_all(send_h, ez, split_axis=0, concat_axis=0, tiled=True)
    recv_meta = lax.all_to_all(send_meta, ez, split_axis=0, concat_axis=0, tiled=True)
    w_pieces = [w_down[0]] + [
        lax.ppermute(w_down[0], "dp", perm=[(i, (i - d) % n_dp) for i in range(n_dp)])
        for d in range(1, n_dp)
    ]
    w_full = jnp.stack(w_pieces)
    dy_z, w_full, recv_h, recv_meta = lax.optimization_barrier((dy_z, w_full, recv_h, recv_meta))
    w_full = jnp.roll(w_full, lax.axis_index("dp"), axis=0).reshape(-1, hid_width)
    dy_pair = lax.ppermute(dy_z, "core", perm=[(c, (c + 1) % n_core) for c in range(n_core)])

    my_core = lax.axis_index("core")
    other_core = (my_core + 1) % n_core

    def inputs(c):
        meta = lax.dynamic_index_in_dim(
            recv_meta.reshape(n_z, n_core, 2, tok_rows), c, axis=1, keepdims=False
        )
        p_c = meta[:, 0, :].reshape(-1)
        slot = meta[:, 1, :].astype(jnp.int32)
        h_src = lax.dynamic_index_in_dim(
            recv_h.reshape(n_z, n_core, slots_per, hid_width), c, axis=1, keepdims=False
        )
        pick = (slot[:, :, None] == jnp.arange(slots_per, dtype=jnp.int32)[None, None, :]).astype(
            h_src.dtype
        )
        h_c = lax.dot_general(
            pick, h_src, (((2,), (1,)), ((0,), (0,))), preferred_element_type=jnp.float32
        ).astype(h_src.dtype)
        return p_c, h_c.reshape(n_z * tok_rows, hid_width)

    p_own, h_own = inputs(my_core)
    p_pair, h_pair = inputs(other_core)

    def part(dy_c, p_c, h_c):
        scaled = (p_c[:, None] * dy_c.astype(jnp.float32)).astype(jnp.bfloat16)
        return lax.dot_general(scaled, h_c, (((0,), (0,)), ((), ())), preferred_element_type=jnp.float32)

    def score(dy_c, h_c):
        g = lax.dot_general(dy_c, w_full, (((1,), (0,)), ((), ())), preferred_element_type=jnp.float32)
        return jnp.sum(g * h_c.astype(jnp.float32), axis=1).reshape(n_z, tok_rows)

    partial = (part(dy_z, p_own, h_own) + part(dy_pair, p_pair, h_pair)).astype(jnp.bfloat16)
    me = lax.axis_index("dp")
    blocks = jnp.roll(partial.reshape(n_dp, -1, hid_width), -me, axis=0)
    grad_block = blocks[0].astype(jnp.float32)
    for d in range(1, n_dp):
        term = lax.ppermute(blocks[d], "dp", perm=[(i, (i + d) % n_dp) for i in range(n_dp)])
        grad_block = grad_block + term.astype(jnp.float32)
    score_own = score(dy_z, h_own)
    score_pair = score(dy_pair, h_pair)

    first = jnp.where(my_core == 0, score_own, score_pair)
    second = jnp.where(my_core == 0, score_pair, score_own)
    by_source = jnp.stack([first, second], axis=1).reshape(groups, tok_rows)
    returned = lax.all_to_all(by_source, ez, split_axis=0, concat_axis=0, tiled=True)
    gate_grad = jnp.sum(
        jnp.where(
            expert_ids[:, :, None] == jnp.arange(groups, dtype=jnp.int32)[None, None, :],
            returned.T[:, None, :],
            jnp.float32(0.0),
        ),
        axis=2,
    )
    return (grad_block[None], gate_grad)


def solution(mesh):
    n_dp, n_expert = mesh.devices.shape
    sub = Mesh(mesh.devices.reshape(n_dp, n_expert // 2, 2), ("dp", "z", "core"))
    tok = ("dp", "z", "core")
    in_specs = (
        P(tok, None, None),
        P(tok, None),
        P(tok, None),
        P(tok, None),
        P(("z", "core"), "dp", None),
    )
    out_specs = (P(("z", "core"), "dp", None), P(tok, None))
    return jax.shard_map(body, mesh=sub, in_specs=in_specs, out_specs=out_specs, check_vma=False)
```

```python
import jax
import jax.numpy as jnp
from jax import lax
from jax.sharding import Mesh, PartitionSpec as P


def body(hidden, upstream, probs, expert_ids, w_down):
    tok_rows, top_k = expert_ids.shape
    hid_width = hidden.shape[2]
    model_width = upstream.shape[1]
    n_z = lax.axis_size("z")
    n_core = lax.axis_size("core")
    n_dp = lax.axis_size("x") * lax.axis_size("y")
    groups = n_z * n_core
    slots_per = max(tok_rows * 9 // 16, tok_rows * top_k // groups)
    total_rows = groups * slots_per
    ez = ("z", "core")

    chosen = (expert_ids[:, :, None] == jnp.arange(groups, dtype=jnp.int32)[None, None, :]).astype(
        jnp.int32
    )
    member = jnp.sum(chosen, axis=1)
    slot_place = jnp.cumsum(member, axis=0) - 1
    which_k = jnp.sum(chosen * jnp.arange(top_k, dtype=jnp.int32)[None, :, None], axis=1)
    target = (
        (member == 1)[:, :, None]
        & (slot_place[:, :, None] == jnp.arange(slots_per, dtype=jnp.int32)[None, None, :])
    ).astype(jnp.int32)
    filled = jnp.sum(target, axis=0) == 1
    source_tok = jnp.sum(target * jnp.arange(tok_rows, dtype=jnp.int32)[:, None, None], axis=0)
    source_k = jnp.sum(target * which_k[:, :, None], axis=0)
    flat_index = (source_tok * top_k + source_k).reshape(-1)
    picked_h = hidden.reshape(tok_rows * top_k, hid_width)[flat_index].reshape(
        groups, slots_per, hid_width
    )
    send_h = jnp.where(filled[:, :, None], picked_h, jnp.zeros_like(picked_h))
    routed = member == 1
    p_tok = jnp.sum(
        jnp.where(chosen == 1, probs.astype(jnp.float32)[:, :, None], jnp.float32(0.0)), axis=1
    )
    inv = jnp.where(routed, slot_place, -1).astype(jnp.float32)
    send_meta = jnp.stack([p_tok.T, inv.T], axis=1)

    dy_z = lax.all_gather(upstream, "z", axis=0, tiled=True)
    recv_h = lax.all_to_all(send_h, ez, split_axis=0, concat_axis=0, tiled=True)
    recv_meta = lax.all_to_all(send_meta, ez, split_axis=0, concat_axis=0, tiled=True)
    def ring_gather(x, axis):
        n = lax.axis_size(axis)
        got = [x] + [lax.ppermute(x, axis, perm=[(i, (i - d) % n) for i in range(n)]) for d in range(1, n)]
        return jnp.roll(jnp.stack(got), lax.axis_index(axis), axis=0)

    w_full = ring_gather(ring_gather(w_down[0], "y"), "x")
    dy_z, w_full, recv_h, recv_meta = lax.optimization_barrier((dy_z, w_full, recv_h, recv_meta))
    w_full = w_full.reshape(-1, hid_width)
    dy_pair = lax.ppermute(dy_z, "core", perm=[(c, (c + 1) % n_core) for c in range(n_core)])

    my_core = lax.axis_index("core")
    other_core = (my_core + 1) % n_core

    def inputs(c):
        meta = lax.dynamic_index_in_dim(
            recv_meta.reshape(n_z, n_core, 2, tok_rows), c, axis=1, keepdims=False
        )
        p_c = meta[:, 0, :].reshape(-1)
        slot = meta[:, 1, :].astype(jnp.int32)
        h_src = lax.dynamic_index_in_dim(
            recv_h.reshape(n_z, n_core, slots_per, hid_width), c, axis=1, keepdims=False
        )
        pick = (slot[:, :, None] == jnp.arange(slots_per, dtype=jnp.int32)[None, None, :]).astype(
            h_src.dtype
        )
        h_c = lax.dot_general(
            pick, h_src, (((2,), (1,)), ((0,), (0,))), preferred_element_type=jnp.float32
        ).astype(h_src.dtype)
        return p_c, h_c.reshape(n_z * tok_rows, hid_width)

    p_own, h_own = inputs(my_core)
    p_pair, h_pair = inputs(other_core)

    def part(dy_c, p_c, h_c):
        scaled = (p_c[:, None] * dy_c.astype(jnp.float32)).astype(jnp.bfloat16)
        return lax.dot_general(scaled, h_c, (((0,), (0,)), ((), ())), preferred_element_type=jnp.float32)

    def score(dy_c, h_c):
        g = lax.dot_general(dy_c, w_full, (((1,), (0,)), ((), ())), preferred_element_type=jnp.float32)
        return jnp.sum(g * h_c.astype(jnp.float32), axis=1).reshape(n_z, tok_rows)

    partial = (part(dy_z, p_own, h_own) + part(dy_pair, p_pair, h_pair)).astype(jnp.bfloat16)
    grad_block = lax.psum_scatter(partial, ("x", "y"), scatter_dimension=0, tiled=True).astype(jnp.float32)
    score_own = score(dy_z, h_own)
    score_pair = score(dy_pair, h_pair)

    first = jnp.where(my_core == 0, score_own, score_pair)
    second = jnp.where(my_core == 0, score_pair, score_own)
    by_source = jnp.stack([first, second], axis=1).reshape(groups, tok_rows)
    returned = lax.all_to_all(by_source, ez, split_axis=0, concat_axis=0, tiled=True)
    gate_grad = jnp.sum(
        jnp.where(
            expert_ids[:, :, None] == jnp.arange(groups, dtype=jnp.int32)[None, None, :],
            returned.T[:, None, :],
            jnp.float32(0.0),
        ),
        axis=2,
    )
    return (grad_block[None], gate_grad)


def solution(mesh):
    n_dp, n_expert = mesh.devices.shape
    side = 4 if n_dp % 4 == 0 else 1
    sub = Mesh(
        mesh.devices.reshape(n_dp // side, side, n_expert // 2, 2), ("x", "y", "z", "core")
    )
    tok = ("x", "y", "z", "core")
    in_specs = (
        P(tok, None, None),
        P(tok, None),
        P(tok, None),
        P(tok, None),
        P(("z", "core"), ("x", "y"), None),
    )
    out_specs = (P(("z", "core"), ("x", "y"), None), P(tok, None))
    return jax.shard_map(body, mesh=sub, in_specs=in_specs, out_specs=out_specs, check_vma=False)
```

```python
import jax
import jax.numpy as jnp
from jax import lax
from jax.sharding import Mesh, PartitionSpec as P


def body(hidden, upstream, probs, expert_ids, w_down):
    tok_rows, top_k = expert_ids.shape
    hid_width = hidden.shape[2]
    model_width = upstream.shape[1]
    n_z = lax.axis_size("z")
    n_core = lax.axis_size("core")
    n_dp = lax.axis_size("x") * lax.axis_size("y")
    groups = n_z * n_core
    slots_per = max(tok_rows * 9 // 16, tok_rows * top_k // groups)
    total_rows = groups * slots_per
    ez = ("z", "core")

    chosen = (expert_ids[:, :, None] == jnp.arange(groups, dtype=jnp.int32)[None, None, :]).astype(
        jnp.int32
    )
    member = jnp.sum(chosen, axis=1)
    slot_place = jnp.cumsum(member, axis=0) - 1
    which_k = jnp.sum(chosen * jnp.arange(top_k, dtype=jnp.int32)[None, :, None], axis=1)
    target = (
        (member == 1)[:, :, None]
        & (slot_place[:, :, None] == jnp.arange(slots_per, dtype=jnp.int32)[None, None, :])
    ).astype(jnp.int32)
    filled = jnp.sum(target, axis=0) == 1
    source_tok = jnp.sum(target * jnp.arange(tok_rows, dtype=jnp.int32)[:, None, None], axis=0)
    source_k = jnp.sum(target * which_k[:, :, None], axis=0)
    flat_index = (source_tok * top_k + source_k).reshape(-1)
    picked_h = hidden.reshape(tok_rows * top_k, hid_width)[flat_index].reshape(
        groups, slots_per, hid_width
    )
    send_h = jnp.where(filled[:, :, None], picked_h, jnp.zeros_like(picked_h))
    routed = member == 1
    p_tok = jnp.sum(
        jnp.where(chosen == 1, probs.astype(jnp.float32)[:, :, None], jnp.float32(0.0)), axis=1
    )
    inv = jnp.where(routed, slot_place, -1).astype(jnp.float32)
    send_meta = jnp.stack([p_tok.T, inv.T], axis=1)

    dy_z = lax.all_gather(upstream, "z", axis=0, tiled=True)
    recv_h = lax.all_to_all(send_h, ez, split_axis=0, concat_axis=0, tiled=True)
    recv_meta = lax.all_to_all(send_meta, ez, split_axis=0, concat_axis=0, tiled=True)
    def ring_gather(x, axis):
        n = lax.axis_size(axis)
        got = [x] + [lax.ppermute(x, axis, perm=[(i, (i - d) % n) for i in range(n)]) for d in range(1, n)]
        return jnp.roll(jnp.stack(got), lax.axis_index(axis), axis=0)

    w_full = ring_gather(ring_gather(w_down[0], "y"), "x")
    my_core = lax.axis_index("core")
    other_core = (my_core + 1) % n_core

    def inputs(c):
        meta = lax.dynamic_index_in_dim(
            recv_meta.reshape(n_z, n_core, 2, tok_rows), c, axis=1, keepdims=False
        )
        p_c = meta[:, 0, :].reshape(-1)
        slot = meta[:, 1, :].astype(jnp.int32)
        h_src = lax.dynamic_index_in_dim(
            recv_h.reshape(n_z, n_core, slots_per, hid_width), c, axis=1, keepdims=False
        )
        pick = (slot[:, :, None] == jnp.arange(slots_per, dtype=jnp.int32)[None, None, :]).astype(
            h_src.dtype
        )
        h_c = lax.dot_general(
            pick, h_src, (((2,), (1,)), ((0,), (0,))), preferred_element_type=jnp.float32
        ).astype(h_src.dtype)
        return p_c, h_c.reshape(n_z * tok_rows, hid_width)

    p_own, h_own = inputs(my_core)
    p_pair, h_pair = inputs(other_core)

    dy_z, w_full, p_own, h_own, p_pair, h_pair = lax.optimization_barrier(
        (dy_z, w_full, p_own, h_own, p_pair, h_pair)
    )
    w_full = w_full.reshape(-1, hid_width)
    dy_pair = lax.ppermute(dy_z, "core", perm=[(c, (c + 1) % n_core) for c in range(n_core)])

    def part(dy_c, p_c, h_c):
        scaled = (p_c[:, None] * dy_c.astype(jnp.float32)).astype(jnp.bfloat16)
        return lax.dot_general(scaled, h_c, (((0,), (0,)), ((), ())), preferred_element_type=jnp.float32)

    def score(dy_c, h_c):
        g = lax.dot_general(dy_c, w_full, (((1,), (0,)), ((), ())), preferred_element_type=jnp.float32)
        return jnp.sum(g * h_c.astype(jnp.float32), axis=1).reshape(n_z, tok_rows)

    partial = (part(dy_z, p_own, h_own) + part(dy_pair, p_pair, h_pair)).astype(jnp.bfloat16)
    grad_block = lax.psum_scatter(partial, ("x", "y"), scatter_dimension=0, tiled=True).astype(jnp.float32)
    score_own = score(dy_z, h_own)
    score_pair = score(dy_pair, h_pair)

    first = jnp.where(my_core == 0, score_own, score_pair)
    second = jnp.where(my_core == 0, score_pair, score_own)
    by_source = jnp.stack([first, second], axis=1).reshape(groups, tok_rows)
    returned = lax.all_to_all(by_source, ez, split_axis=0, concat_axis=0, tiled=True)
    gate_grad = jnp.sum(
        jnp.where(
            expert_ids[:, :, None] == jnp.arange(groups, dtype=jnp.int32)[None, None, :],
            returned.T[:, None, :],
            jnp.float32(0.0),
        ),
        axis=2,
    )
    return (grad_block[None], gate_grad)


def solution(mesh):
    n_dp, n_expert = mesh.devices.shape
    side = 4 if n_dp % 4 == 0 else 1
    sub = Mesh(
        mesh.devices.reshape(n_dp // side, side, n_expert // 2, 2), ("x", "y", "z", "core")
    )
    tok = ("x", "y", "z", "core")
    in_specs = (
        P(tok, None, None),
        P(tok, None),
        P(tok, None),
        P(tok, None),
        P(("z", "core"), ("x", "y"), None),
    )
    out_specs = (P(("z", "core"), ("x", "y"), None), P(tok, None))
    return jax.shard_map(body, mesh=sub, in_specs=in_specs, out_specs=out_specs, check_vma=False)
```

```python
import jax
import jax.numpy as jnp
from jax import lax
from jax.sharding import Mesh, PartitionSpec as P


def body(hidden, upstream, probs, expert_ids, w_down):
    tok_rows, top_k = expert_ids.shape
    hid_width = hidden.shape[2]
    model_width = upstream.shape[1]
    n_z = lax.axis_size("z")
    n_core = lax.axis_size("core")
    n_dp = lax.axis_size("x") * lax.axis_size("y")
    groups = n_z * n_core
    slots_per = max(tok_rows * 9 // 16, tok_rows * top_k // groups)
    total_rows = groups * slots_per
    ez = ("z", "core")

    chosen = (expert_ids[:, :, None] == jnp.arange(groups, dtype=jnp.int32)[None, None, :]).astype(
        jnp.int32
    )
    member = jnp.sum(chosen, axis=1)
    slot_place = jnp.cumsum(member, axis=0) - 1
    which_k = jnp.sum(chosen * jnp.arange(top_k, dtype=jnp.int32)[None, :, None], axis=1)
    target = (
        (member == 1)[:, :, None]
        & (slot_place[:, :, None] == jnp.arange(slots_per, dtype=jnp.int32)[None, None, :])
    ).astype(jnp.int32)
    filled = jnp.sum(target, axis=0) == 1
    source_tok = jnp.sum(target * jnp.arange(tok_rows, dtype=jnp.int32)[:, None, None], axis=0)
    source_k = jnp.sum(target * which_k[:, :, None], axis=0)
    flat_index = (source_tok * top_k + source_k).reshape(-1)
    picked_h = hidden.reshape(tok_rows * top_k, hid_width)[flat_index].reshape(
        groups, slots_per, hid_width
    )
    send_h = jnp.where(filled[:, :, None], picked_h, jnp.zeros_like(picked_h))
    routed = member == 1
    p_tok = jnp.sum(
        jnp.where(chosen == 1, probs.astype(jnp.float32)[:, :, None], jnp.float32(0.0)), axis=1
    )
    inv = jnp.where(routed, slot_place, -1).astype(jnp.float32)
    send_meta = jnp.stack([p_tok.T, inv.T], axis=1)

    dy_z = lax.all_gather(upstream, "z", axis=0, tiled=True)
    mine = lax.axis_index("core")
    by_core = send_h.reshape(n_z, n_core, slots_per, hid_width)
    for_pair = lax.dynamic_index_in_dim(by_core, (mine + 1) % n_core, axis=1, keepdims=False)
    for_me = lax.dynamic_index_in_dim(by_core, mine, axis=1, keepdims=False)
    from_pair = lax.ppermute(for_pair, "core", perm=[(c, (c + 1) % n_core) for c in range(n_core)])
    recv_h = lax.all_to_all(
        jnp.stack([for_me, from_pair], axis=1), "z", split_axis=0, concat_axis=0, tiled=True
    )
    recv_meta = lax.all_to_all(send_meta, ez, split_axis=0, concat_axis=0, tiled=True)
    def ring_gather(x, axis):
        n = lax.axis_size(axis)
        got = [x] + [lax.ppermute(x, axis, perm=[(i, (i - d) % n) for i in range(n)]) for d in range(1, n)]
        return jnp.roll(jnp.stack(got), lax.axis_index(axis), axis=0)

    w_full = ring_gather(ring_gather(w_down[0], "y"), "x")
    dy_z, w_full, recv_h, recv_meta = lax.optimization_barrier((dy_z, w_full, recv_h, recv_meta))
    w_full = w_full.reshape(-1, hid_width)
    dy_pair = lax.ppermute(dy_z, "core", perm=[(c, (c + 1) % n_core) for c in range(n_core)])

    my_core = lax.axis_index("core")
    other_core = (my_core + 1) % n_core

    def inputs(c, own):
        meta = lax.dynamic_index_in_dim(
            recv_meta.reshape(n_z, n_core, 2, tok_rows), c, axis=1, keepdims=False
        )
        p_c = meta[:, 0, :].reshape(-1)
        slot = meta[:, 1, :].astype(jnp.int32)
        h_src = recv_h[:, 0] if own else recv_h[:, 1]
        pick = (slot[:, :, None] == jnp.arange(slots_per, dtype=jnp.int32)[None, None, :]).astype(
            h_src.dtype
        )
        h_c = lax.dot_general(
            pick, h_src, (((2,), (1,)), ((0,), (0,))), preferred_element_type=jnp.float32
        ).astype(h_src.dtype)
        return p_c, h_c.reshape(n_z * tok_rows, hid_width)

    p_own, h_own = inputs(my_core, True)
    p_pair, h_pair = inputs(other_core, False)

    def part(dy_c, p_c, h_c):
        scaled = (p_c[:, None] * dy_c.astype(jnp.float32)).astype(jnp.bfloat16)
        return lax.dot_general(scaled, h_c, (((0,), (0,)), ((), ())), preferred_element_type=jnp.float32)

    def score(dy_c, h_c):
        g = lax.dot_general(dy_c, w_full, (((1,), (0,)), ((), ())), preferred_element_type=jnp.float32)
        return jnp.sum(g * h_c.astype(jnp.float32), axis=1).reshape(n_z, tok_rows)

    partial = (part(dy_z, p_own, h_own) + part(dy_pair, p_pair, h_pair)).astype(jnp.bfloat16)
    grad_block = lax.psum_scatter(partial, ("x", "y"), scatter_dimension=0, tiled=True).astype(jnp.float32)
    score_own = score(dy_z, h_own)
    score_pair = score(dy_pair, h_pair)

    first = jnp.where(my_core == 0, score_own, score_pair)
    second = jnp.where(my_core == 0, score_pair, score_own)
    by_source = jnp.stack([first, second], axis=1).reshape(groups, tok_rows)
    returned = lax.all_to_all(by_source, ez, split_axis=0, concat_axis=0, tiled=True)
    gate_grad = jnp.sum(
        jnp.where(
            expert_ids[:, :, None] == jnp.arange(groups, dtype=jnp.int32)[None, None, :],
            returned.T[:, None, :],
            jnp.float32(0.0),
        ),
        axis=2,
    )
    return (grad_block[None], gate_grad)


def solution(mesh):
    n_dp, n_expert = mesh.devices.shape
    side = 4 if n_dp % 4 == 0 else 1
    sub = Mesh(
        mesh.devices.reshape(n_dp // side, side, n_expert // 2, 2), ("x", "y", "z", "core")
    )
    tok = ("x", "y", "z", "core")
    in_specs = (
        P(tok, None, None),
        P(tok, None),
        P(tok, None),
        P(tok, None),
        P(("z", "core"), ("x", "y"), None),
    )
    out_specs = (P(("z", "core"), ("x", "y"), None), P(tok, None))
    return jax.shard_map(body, mesh=sub, in_specs=in_specs, out_specs=out_specs, check_vma=False)
```

```python
import jax
import jax.numpy as jnp
from jax import lax
from jax.sharding import Mesh, PartitionSpec as P


def body(hidden, upstream, probs, expert_ids, w_down):
    tok_rows, top_k = expert_ids.shape
    hid_width = hidden.shape[2]
    model_width = upstream.shape[1]
    n_z = lax.axis_size("z")
    n_core = lax.axis_size("core")
    n_dp = lax.axis_size("x") * lax.axis_size("y")
    groups = n_z * n_core
    slots_per = max(tok_rows * 9 // 16, tok_rows * top_k // groups)
    total_rows = groups * slots_per
    ez = ("z", "core")

    chosen = (expert_ids[:, :, None] == jnp.arange(groups, dtype=jnp.int32)[None, None, :]).astype(
        jnp.int32
    )
    member = jnp.sum(chosen, axis=1)
    slot_place = jnp.cumsum(member, axis=0) - 1
    which_k = jnp.sum(chosen * jnp.arange(top_k, dtype=jnp.int32)[None, :, None], axis=1)
    target = (
        (member == 1)[:, :, None]
        & (slot_place[:, :, None] == jnp.arange(slots_per, dtype=jnp.int32)[None, None, :])
    ).astype(jnp.int32)
    filled = jnp.sum(target, axis=0) == 1
    source_tok = jnp.sum(target * jnp.arange(tok_rows, dtype=jnp.int32)[:, None, None], axis=0)
    source_k = jnp.sum(target * which_k[:, :, None], axis=0)
    flat_index = (source_tok * top_k + source_k).reshape(-1)
    picked_h = hidden.reshape(tok_rows * top_k, hid_width)[flat_index].reshape(
        groups, slots_per, hid_width
    )
    send_h = jnp.where(filled[:, :, None], picked_h, jnp.zeros_like(picked_h))
    routed = member == 1
    p_tok = jnp.sum(
        jnp.where(chosen == 1, probs.astype(jnp.float32)[:, :, None], jnp.float32(0.0)), axis=1
    )
    inv = jnp.where(routed, slot_place, -1).astype(jnp.float32)
    send_meta = jnp.stack([p_tok.T, inv.T], axis=1)

    dy_z = lax.all_gather(upstream, "z", axis=0, tiled=True)
    recv_h = lax.all_to_all(send_h, ez, split_axis=0, concat_axis=0, tiled=True)
    recv_h, send_meta = lax.optimization_barrier((recv_h, send_meta))
    recv_meta = lax.all_to_all(send_meta, ez, split_axis=0, concat_axis=0, tiled=True)
    def ring_gather(x, axis):
        n = lax.axis_size(axis)
        got = [x] + [lax.ppermute(x, axis, perm=[(i, (i - d) % n) for i in range(n)]) for d in range(1, n)]
        return jnp.roll(jnp.stack(got), lax.axis_index(axis), axis=0)

    w_full = ring_gather(ring_gather(w_down[0], "y"), "x")
    dy_z, w_full, recv_h, recv_meta = lax.optimization_barrier((dy_z, w_full, recv_h, recv_meta))
    w_full = w_full.reshape(-1, hid_width)
    dy_pair = lax.ppermute(dy_z, "core", perm=[(c, (c + 1) % n_core) for c in range(n_core)])

    my_core = lax.axis_index("core")
    other_core = (my_core + 1) % n_core

    def inputs(c):
        meta = lax.dynamic_index_in_dim(
            recv_meta.reshape(n_z, n_core, 2, tok_rows), c, axis=1, keepdims=False
        )
        p_c = meta[:, 0, :].reshape(-1)
        slot = meta[:, 1, :].astype(jnp.int32)
        h_src = lax.dynamic_index_in_dim(
            recv_h.reshape(n_z, n_core, slots_per, hid_width), c, axis=1, keepdims=False
        )
        pick = (slot[:, :, None] == jnp.arange(slots_per, dtype=jnp.int32)[None, None, :]).astype(
            h_src.dtype
        )
        h_c = lax.dot_general(
            pick, h_src, (((2,), (1,)), ((0,), (0,))), preferred_element_type=jnp.float32
        ).astype(h_src.dtype)
        return p_c, h_c.reshape(n_z * tok_rows, hid_width)

    p_own, h_own = inputs(my_core)
    p_pair, h_pair = inputs(other_core)

    def part(dy_c, p_c, h_c):
        scaled = (p_c[:, None] * dy_c.astype(jnp.float32)).astype(jnp.bfloat16)
        return lax.dot_general(scaled, h_c, (((0,), (0,)), ((), ())), preferred_element_type=jnp.float32)

    def score(dy_c, h_c):
        g = lax.dot_general(dy_c, w_full, (((1,), (0,)), ((), ())), preferred_element_type=jnp.float32)
        return jnp.sum(g * h_c.astype(jnp.float32), axis=1).reshape(n_z, tok_rows)

    partial = (part(dy_z, p_own, h_own) + part(dy_pair, p_pair, h_pair)).astype(jnp.bfloat16)
    grad_block = lax.psum_scatter(partial, ("x", "y"), scatter_dimension=0, tiled=True).astype(jnp.float32)
    score_own = score(dy_z, h_own)
    score_pair = score(dy_pair, h_pair)

    first = jnp.where(my_core == 0, score_own, score_pair)
    second = jnp.where(my_core == 0, score_pair, score_own)
    by_source = jnp.stack([first, second], axis=1).reshape(groups, tok_rows)
    returned = lax.all_to_all(by_source, ez, split_axis=0, concat_axis=0, tiled=True)
    gate_grad = jnp.sum(
        jnp.where(
            expert_ids[:, :, None] == jnp.arange(groups, dtype=jnp.int32)[None, None, :],
            returned.T[:, None, :],
            jnp.float32(0.0),
        ),
        axis=2,
    )
    return (grad_block[None], gate_grad)


def solution(mesh):
    n_dp, n_expert = mesh.devices.shape
    side = 4 if n_dp % 4 == 0 else 1
    sub = Mesh(
        mesh.devices.reshape(n_dp // side, side, n_expert // 2, 2), ("x", "y", "z", "core")
    )
    tok = ("x", "y", "z", "core")
    in_specs = (
        P(tok, None, None),
        P(tok, None),
        P(tok, None),
        P(tok, None),
        P(("z", "core"), ("x", "y"), None),
    )
    out_specs = (P(("z", "core"), ("x", "y"), None), P(tok, None))
    return jax.shard_map(body, mesh=sub, in_specs=in_specs, out_specs=out_specs, check_vma=False)
```
